512 devices in a mesh: fsdp: 64 (over y, x, core), tp: 8 (over z).
Axes of the slice: x: 4, y: 8, z: 8, core: 2. Of those that a mesh axis runs over, the one named last changes fastest.
Arguments:
- grads: bfloat16 [2, 12288, 2560], P(None, 'fsdp', 'tp'), may hold values from -16 to 16
- weights: float32 [2, 12288, 2560], P(None, 'fsdp', 'tp'), may hold values from -0.3 to 0.3
- basis: bfloat16 [2560, 2, 256], P('tp'), may hold values from -0.375 to 0.375
- first_moment: float32 [2, 12288, 256], P(None, 'fsdp', 'tp'), may hold values from -12 to 12
- second_moment: float32 [2, 12288, 256], P(None, 'fsdp', 'tp'), may hold values from 0.05 to 5
Outputs:
- weight_next: float32 [2, 12288, 2560], P(None, 'fsdp', 'tp')
- first_next: float32 [2, 12288, 256], P(None, 'fsdp', 'tp')
- second_next: float32 [2, 12288, 256], P(None, 'fsdp', 'tp')
- basis_next: bfloat16 [2560, 2, 256], P('tp')
The draws below stay inside these ranges and needn't reach their ends.
All inputs are finite; a program needn't handle non-finite values.
Results may differ from the reference program's by a relative error of at most 0.0034.
Values may be sent and summed in bfloat16 or wider, within the bound.
No kernel may reach another device: no remote copies, remote signals or barrier semaphores. Data moves between devices by JAX's collectives and lax.ppermute only.
A program may use at most 64 MiB of HBM per device.

```python
import math
import jax
import jax.numpy as jnp
from jax import lax

D = 2560
FF = 12288
RANK = 256
MATS = 2


def strengthened(values, stream_key, source, target, shards_of, factor):
    def block_of(dim):
        return (jnp.arange(values.shape[dim]) // (values.shape[dim] // shards_of)).reshape((-1,) + (1,) * (values.ndim - 1 - dim))

    one_side = jax.random.permutation(stream_key, shards_of)[block_of(target)]
    far = (block_of(target) + shards_of // 2) % shards_of
    return jnp.where((block_of(source) == one_side) | (block_of(source) == far), factor * values, values)


def block_scale(own_key, shape, pieces, low, largest):
    def one(position, parts):
        draws = jax.random.uniform(jax.random.fold_in(jax.random.fold_in(own_key, 6), position), (parts,), jnp.float32, low / len(pieces), largest / len(pieces))
        return jnp.repeat(jnp.exp(draws), shape[position] // parts).reshape((-1,) + (1,) * (len(shape) - position - 1))

    loudness = one(*pieces[0])
    for cut in pieces[1:]:
        loudness = loudness * one(*cut)
    return loudness


def noise(key, dims, scale, most, split=(), kind=jnp.bfloat16):
    loudness = block_scale(key, dims, split, -0.22, 0.18) if split else 1.0
    values = jax.random.normal(key, dims, jnp.float32) * scale * loudness
    return jnp.minimum(jnp.maximum(values, -most), most).astype(kind)


def bell_draw_with(key, shape, scale, reach, cuts, heavy, kind=jnp.bfloat16):
    array = scale * jax.random.normal(key, shape, jnp.float32)
    if cuts:
        array = array * block_scale(key, shape, cuts, -0.22, 0.18)
    return jnp.clip(strengthened(array, jax.random.fold_in(key, 3), *heavy), -reach, reach).astype(kind)


def setup_inputs(seed: int = 0) -> dict:
    arg_keys = jax.random.split(jax.random.key(seed), 6)
    return {
        "grads": bell_draw_with(arg_keys[0], (MATS, FF, D), 1.0, 16.0, ((1, 64), (2, 8)), (1, 2, 64, 4.0)),
        "weights": noise(arg_keys[1], (MATS, FF, D), 0.05, 0.3, ((1, 64), (2, 8)), jnp.float32),
        "basis": noise(arg_keys[2], (D, MATS, RANK), RANK ** -0.5, 0.375, ((0, 8),)),
        "first_moment": noise(arg_keys[3], (MATS, FF, RANK), 2.0, 12.0, ((1, 64), (2, 8)), jnp.float32),
        "second_moment": jnp.clip(jnp.exp(math.log(5.0) - 4.6051702 * jax.random.uniform(arg_keys[4], (MATS, FF, RANK), jnp.float32) ** block_scale(arg_keys[4], (MATS, FF, RANK), ((1, 64), (2, 8)), -0.2, 0.2)), 0.05, 5.0),
    }


BETA_FIRST = 0.9
BETA_SECOND = 0.999
BIAS_FIRST = 0.9999734386011124
BIAS_SECOND = 0.0952078528862904
EPSILON = 1e-08
EPSILON_NORM = 1e-06
LEARNING_RATE = 0.1
GALORE_SCALE = 0.25

def reference(grads, weights, basis, first_moment, second_moment):
    highest = lax.Precision.HIGHEST
    grads_wide = grads.astype(jnp.float32)
    basis_wide = basis.astype(jnp.float32)
    projected = jnp.einsum('mfd,dmr->mfr', grads_wide, basis_wide, precision=highest)
    first_next = BETA_FIRST * first_moment + (1.0 - BETA_FIRST) * projected
    second_next = BETA_SECOND * second_moment + (1.0 - BETA_SECOND) * projected * projected
    normal = first_next / BIAS_FIRST / (jnp.sqrt(second_next / BIAS_SECOND) + EPSILON)
    normal_half = normal.astype(jnp.bfloat16)
    update = jnp.einsum('mfr,dmr->mfd', normal_half.astype(jnp.float32), basis_wide, precision=highest)
    weight_next = weights - LEARNING_RATE * GALORE_SCALE * update
    projected_half = projected.astype(jnp.bfloat16)
    image = jnp.einsum('mfd,mfr->dmr', grads_wide, projected_half.astype(jnp.float32), precision=highest)
    total = lax.optimization_barrier(jnp.sum(image * image, axis=(0, 2))) + EPSILON_NORM
    scaled = image * jnp.sqrt(RANK / total)[None, :, None]
    cross = jnp.einsum('dmr,dms->mrs', scaled, scaled, precision=highest)
    shaped = 1.5 * scaled - 0.5 * jnp.einsum('dmr,mrs->dms', scaled, cross, precision=highest)
    basis_next = (jnp.sqrt(D / RANK) * shaped).astype(jnp.bfloat16)
    return (weight_next, first_next, second_next, basis_next)
```

```python
import jax
import jax.numpy as jnp
from jax import lax
from jax.sharding import PartitionSpec as P

D = 2560


BETA_FIRST = 0.9
BETA_SECOND = 0.999
BIAS_FIRST = 0.9999734386011124
BIAS_SECOND = 0.0952078528862904
EPSILON = 1e-08
EPSILON_NORM = 1e-06
LEARNING_RATE = 0.1
GALORE_SCALE = 0.25


def adam_share(grad_share, first_moment, second_moment):
    first_next = BETA_FIRST * first_moment + (1.0 - BETA_FIRST) * grad_share
    second_next = BETA_SECOND * second_moment + (1.0 - BETA_SECOND) * grad_share * grad_share
    normal = first_next / BIAS_FIRST / (jnp.sqrt(second_next / BIAS_SECOND) + EPSILON)
    return (first_next, second_next, normal.astype(jnp.bfloat16))


def partner_perm(size, bit):
    return [(i, i ^ (1 << bit)) for i in range(size)]


def butterfly_sum(value, axis, size):
    bit = 0
    while (1 << bit) < size:
        value = value + lax.ppermute(value, axis, partner_perm(size, bit))
        bit += 1
    return value


def halving_scatter(value, axis, size, stages):
    index = lax.axis_index(axis)
    for bit, dim in stages:
        half = value.shape[dim] // 2
        mine = (index >> bit) & 1
        keep = lax.dynamic_slice_in_dim(value, mine * half, half, dim)
        send = lax.dynamic_slice_in_dim(value, (1 - mine) * half, half, dim)
        value = keep + lax.ppermute(send, axis, partner_perm(size, bit))
    return value


def doubling_gather(value, axis, size, stages):
    index = lax.axis_index(axis)
    for bit, dim in reversed(stages):
        mine = (index >> bit) & 1
        other = lax.ppermute(value, axis, partner_perm(size, bit))
        low = jnp.where(mine == 0, value, other)
        high = jnp.where(mine == 0, other, value)
        value = jnp.concatenate([low, high], axis=dim)
    return value


def shards(grads, weights, basis, first_moment, second_moment):
    highest = lax.Precision.HIGHEST
    fsdp = lax.axis_size("fsdp")
    tp = lax.axis_size("tp")
    width = first_moment.shape[2]
    rank_width = basis.shape[2]

    projected_part = jnp.einsum("mfd,dmr->mfr", grads, basis, preferred_element_type=jnp.float32)
    projected = butterfly_sum(projected_part, "tp", tp)
    own = lax.dynamic_slice_in_dim(projected, lax.axis_index("tp") * width, width, 2)
    first_next, second_next, normal_half = adam_share(own, first_moment, second_moment)
    projected_half = projected.astype(jnp.bfloat16)

    image_part = jnp.einsum("mfd,mfr->mdr", grads, projected_half, preferred_element_type=jnp.float32)
    stages = [(0, 0), (1, 2), (3, 1), (2, 1), (4, 1), (5, 1)]
    image = doubling_gather(halving_scatter(image_part, "fsdp", fsdp, stages), "fsdp", fsdp, stages)

    tp_bits = [(b, 2) for b in range(tp.bit_length() - 1)]
    normal_full = doubling_gather(normal_half, "tp", tp, list(reversed(tp_bits)))
    update = jnp.einsum("mfr,dmr->mfd", normal_full, basis, preferred_element_type=jnp.float32)
    weight_next = weights - LEARNING_RATE * GALORE_SCALE * update

    gram = butterfly_sum(jnp.einsum("mdr,mds->mrs", image, image, precision=highest), "tp", tp)
    total = jnp.sum(jnp.diagonal(gram, axis1=1, axis2=2), axis=1) + EPSILON_NORM
    factor = jnp.sqrt(rank_width / total)
    scaled = image * factor[:, None, None]
    cross = gram * (factor * factor)[:, None, None]
    shaped = 1.5 * scaled - 0.5 * jnp.einsum("mdr,mrs->mds", scaled, cross, precision=highest)
    basis_next = jnp.transpose((jnp.sqrt(D / rank_width) * shaped).astype(jnp.bfloat16), (1, 0, 2))
    return (weight_next, first_next, second_next, basis_next)


def solution(mesh):
    in_specs = (
        P(None, "fsdp", "tp"),
        P(None, "fsdp", "tp"),
        P("tp", None, None),
        P(None, "fsdp", "tp"),
        P(None, "fsdp", "tp"),
    )
    out_specs = (
        P(None, "fsdp", "tp"),
        P(None, "fsdp", "tp"),
        P(None, "fsdp", "tp"),
        P("tp", None, None),
    )
    return jax.shard_map(shards, mesh=mesh, in_specs=in_specs, out_specs=out_specs, check_vma=False)
```

```python
import jax
import jax.numpy as jnp
from jax import lax
from jax.sharding import PartitionSpec as P

D = 2560


BETA_FIRST = 0.9
BETA_SECOND = 0.999
BIAS_FIRST = 0.9999734386011124
BIAS_SECOND = 0.0952078528862904
EPSILON = 1e-08
EPSILON_NORM = 1e-06
LEARNING_RATE = 0.1
GALORE_SCALE = 0.25


def adam_share(grad_share, first_moment, second_moment):
    first_next = BETA_FIRST * first_moment + (1.0 - BETA_FIRST) * grad_share
    second_next = BETA_SECOND * second_moment + (1.0 - BETA_SECOND) * grad_share * grad_share
    normal = first_next / BIAS_FIRST / (jnp.sqrt(second_next / BIAS_SECOND) + EPSILON)
    return (first_next, second_next, normal.astype(jnp.bfloat16))


def partner_perm(size, bit):
    return [(i, i ^ (1 << bit)) for i in range(size)]


def butterfly_sum(value, axis, size):
    bit = 0
    while (1 << bit) < size:
        value = value + lax.ppermute(value, axis, partner_perm(size, bit))
        bit += 1
    return value


def halving_scatter(value, axis, size, stages):
    index = lax.axis_index(axis)
    for bit, dim in stages:
        half = value.shape[dim] // 2
        mine = (index >> bit) & 1
        keep = lax.dynamic_slice_in_dim(value, mine * half, half, dim)
        send = lax.dynamic_slice_in_dim(value, (1 - mine) * half, half, dim)
        value = keep + lax.ppermute(send, axis, partner_perm(size, bit))
    return value


def doubling_gather(value, axis, size, stages):
    index = lax.axis_index(axis)
    for bit, dim in reversed(stages):
        mine = (index >> bit) & 1
        other = lax.ppermute(value, axis, partner_perm(size, bit))
        low = jnp.where(mine == 0, value, other)
        high = jnp.where(mine == 0, other, value)
        value = jnp.concatenate([low, high], axis=dim)
    return value


def reverse_blocks(value, bits, width):
    lead = value.shape[:-1]
    split = value.reshape(lead + (2,) * bits + (width,))
    axes = tuple(range(len(lead))) + tuple(len(lead) + bits - 1 - i for i in range(bits)) + (len(lead) + bits,)
    return jnp.transpose(split, axes).reshape(value.shape)


def shards(grads, weights, basis, first_moment, second_moment):
    highest = lax.Precision.HIGHEST
    fsdp = lax.axis_size("fsdp")
    tp = lax.axis_size("tp")
    width = first_moment.shape[2]
    rank_width = basis.shape[2]
    tp_bits = [(b, 2) for b in range(tp.bit_length() - 1)]
    basis_order = reverse_blocks(basis, len(tp_bits), width)

    projected_part = jnp.einsum("mfd,dmr->mfr", grads, basis_order, preferred_element_type=jnp.float32)
    own = halving_scatter(projected_part, "tp", tp, tp_bits)
    first_next, second_next, normal_half = adam_share(own, first_moment, second_moment)
    halves = jnp.stack([own.astype(jnp.bfloat16), normal_half], axis=0)
    gathered = doubling_gather(halves, "tp", tp, [(b, 3) for b, _ in tp_bits])
    projected_half, normal_full = gathered[0], gathered[1]

    image_part = jnp.einsum("mfd,mfr->mdr", grads, projected_half, preferred_element_type=jnp.float32)
    stages = [(0, 0), (1, 2), (3, 1), (2, 1), (4, 1), (5, 1)]
    image = doubling_gather(halving_scatter(image_part, "fsdp", fsdp, stages), "fsdp", fsdp, stages)

    update = jnp.einsum("mfr,dmr->mfd", normal_full, basis_order, preferred_element_type=jnp.float32)
    weight_next = weights - LEARNING_RATE * GALORE_SCALE * update

    gram = butterfly_sum(jnp.einsum("mdr,mds->mrs", image, image, precision=highest), "tp", tp)
    diagonal = lax.broadcasted_iota(jnp.int32, gram.shape, 1) == lax.broadcasted_iota(jnp.int32, gram.shape, 2)
    total = jnp.sum(jnp.where(diagonal, gram, 0.0), axis=(1, 2)) + EPSILON_NORM
    factor = jnp.sqrt(rank_width / total)
    scaled = image * factor[:, None, None]
    cross = gram * (factor * factor)[:, None, None]
    shaped = 1.5 * scaled - 0.5 * jnp.einsum("mdr,mrs->mds", scaled, cross, precision=highest)
    basis_next = reverse_blocks((jnp.sqrt(D / rank_width) * shaped).astype(jnp.bfloat16), len(tp_bits), width)
    return (weight_next, first_next, second_next, jnp.transpose(basis_next, (1, 0, 2)))


def solution(mesh):
    in_specs = (
        P(None, "fsdp", "tp"),
        P(None, "fsdp", "tp"),
        P("tp", None, None),
        P(None, "fsdp", "tp"),
        P(None, "fsdp", "tp"),
    )
    out_specs = (
        P(None, "fsdp", "tp"),
        P(None, "fsdp", "tp"),
        P(None, "fsdp", "tp"),
        P("tp", None, None),
    )
    return jax.shard_map(shards, mesh=mesh, in_specs=in_specs, out_specs=out_specs, check_vma=False)
```

```python
import jax
import jax.numpy as jnp
from jax import lax
from jax.sharding import PartitionSpec as P

D = 2560


BETA_FIRST = 0.9
BETA_SECOND = 0.999
BIAS_FIRST = 0.9999734386011124
BIAS_SECOND = 0.0952078528862904
EPSILON = 1e-08
EPSILON_NORM = 1e-06
LEARNING_RATE = 0.1
GALORE_SCALE = 0.25


def adam_share(grad_share, first_moment, second_moment):
    first_next = BETA_FIRST * first_moment + (1.0 - BETA_FIRST) * grad_share
    second_next = BETA_SECOND * second_moment + (1.0 - BETA_SECOND) * grad_share * grad_share
    normal = first_next / BIAS_FIRST / (jnp.sqrt(second_next / BIAS_SECOND) + EPSILON)
    return (first_next, second_next, normal.astype(jnp.bfloat16))


def partner_perm(size, bit):
    return [(i, i ^ (1 << bit)) for i in range(size)]


def butterfly_sum(value, axis, size):
    bit = 0
    while (1 << bit) < size:
        value = value + lax.ppermute(value, axis, partner_perm(size, bit))
        bit += 1
    return value


def halving_scatter(value, axis, size, stages):
    index = lax.axis_index(axis)
    for bit, dim in stages:
        half = value.shape[dim] // 2
        mine = (index >> bit) & 1
        keep = lax.dynamic_slice_in_dim(value, mine * half, half, dim)
        send = lax.dynamic_slice_in_dim(value, (1 - mine) * half, half, dim)
        value = keep + lax.ppermute(send, axis, partner_perm(size, bit))
    return value


def doubling_gather(value, axis, size, stages):
    index = lax.axis_index(axis)
    for bit, dim in reversed(stages):
        mine = (index >> bit) & 1
        other = lax.ppermute(value, axis, partner_perm(size, bit))
        low = jnp.where(mine == 0, value, other)
        high = jnp.where(mine == 0, other, value)
        value = jnp.concatenate([low, high], axis=dim)
    return value


def reverse_blocks(value, bits, width):
    lead = value.shape[:-1]
    split = value.reshape(lead + (2,) * bits + (width,))
    axes = tuple(range(len(lead))) + tuple(len(lead) + bits - 1 - i for i in range(bits)) + (len(lead) + bits,)
    return jnp.transpose(split, axes).reshape(value.shape)


def block_masks(shape):
    rows = lax.broadcasted_iota(jnp.int32, shape, 1)
    cols = lax.broadcasted_iota(jnp.int32, shape, 2)
    return rows < cols, rows == cols, rows > cols


def pack_gram(gram):
    h = gram.shape[1] // 2
    top_left, top_right, bottom_right = gram[:, :h, :h], gram[:, :h, h:], gram[:, h:, h:]
    upper, same, lower = block_masks(top_left.shape)
    folded = jnp.where(upper | same, top_left, bottom_right)
    corner = jnp.sum(jnp.where(same, bottom_right, 0.0), axis=1, keepdims=True)
    return jnp.concatenate([folded, top_right, corner], axis=1)


def unpack_gram(packed):
    h = packed.shape[2]
    folded, top_right, corner = packed[:, :h], packed[:, h : 2 * h], packed[:, 2 * h :]
    upper, same, lower = block_masks(folded.shape)
    flipped = jnp.transpose(folded, (0, 2, 1))
    top_left = jnp.where(upper | same, folded, flipped)
    bottom_right = jnp.where(lower, folded, jnp.where(same, corner, flipped))
    top = jnp.concatenate([top_left, top_right], axis=2)
    bottom = jnp.concatenate([jnp.transpose(top_right, (0, 2, 1)), bottom_right], axis=2)
    return jnp.concatenate([top, bottom], axis=1)


def shards(grads, weights, basis, first_moment, second_moment):
    highest = lax.Precision.HIGHEST
    fsdp = lax.axis_size("fsdp")
    tp = lax.axis_size("tp")
    width = first_moment.shape[2]
    rank_width = basis.shape[2]
    tp_bits = [(b, 2) for b in range(tp.bit_length() - 1)]
    basis_order = reverse_blocks(basis, len(tp_bits), width)

    projected_part = jnp.einsum("mfd,dmr->mfr", grads, basis_order, preferred_element_type=jnp.float32)
    own = halving_scatter(projected_part, "tp", tp, tp_bits)
    first_next, second_next, normal_half = adam_share(own, first_moment, second_moment)
    halves = jnp.stack([own.astype(jnp.bfloat16), normal_half], axis=0)
    gathered = doubling_gather(halves, "tp", tp, [(b, 3) for b, _ in tp_bits])
    projected_half, normal_full = gathered[0], gathered[1]

    image_part = jnp.einsum("mfd,mfr->mdr", grads, projected_half, preferred_element_type=jnp.float32)
    stages = [(0, 0), (1, 2), (3, 1), (2, 1), (4, 1), (5, 1)]
    image = doubling_gather(halving_scatter(image_part, "fsdp", fsdp, stages), "fsdp", fsdp, stages)

    update = jnp.einsum("mfr,dmr->mfd", normal_full, basis_order, preferred_element_type=jnp.float32)
    weight_next = weights - LEARNING_RATE * GALORE_SCALE * update

    gram = unpack_gram(butterfly_sum(pack_gram(jnp.einsum("mdr,mds->mrs", image, image, precision=highest)), "tp", tp))
    diagonal = lax.broadcasted_iota(jnp.int32, gram.shape, 1) == lax.broadcasted_iota(jnp.int32, gram.shape, 2)
    total = jnp.sum(jnp.where(diagonal, gram, 0.0), axis=(1, 2)) + EPSILON_NORM
    factor = jnp.sqrt(rank_width / total)
    scaled = image * factor[:, None, None]
    cross = gram * (factor * factor)[:, None, None]
    shaped = 1.5 * scaled - 0.5 * jnp.einsum("mdr,mrs->mds", scaled, cross, precision=highest)
    basis_next = reverse_blocks((jnp.sqrt(D / rank_width) * shaped).astype(jnp.bfloat16), len(tp_bits), width)
    return (weight_next, first_next, second_next, jnp.transpose(basis_next, (1, 0, 2)))


def solution(mesh):
    in_specs = (
        P(None, "fsdp", "tp"),
        P(None, "fsdp", "tp"),
        P("tp", None, None),
        P(None, "fsdp", "tp"),
        P(None, "fsdp", "tp"),
    )
    out_specs = (
        P(None, "fsdp", "tp"),
        P(None, "fsdp", "tp"),
        P(None, "fsdp", "tp"),
        P("tp", None, None),
    )
    return jax.shard_map(shards, mesh=mesh, in_specs=in_specs, out_specs=out_specs, check_vma=False)
```

```python
import jax
import jax.numpy as jnp
from jax import lax
from jax.sharding import PartitionSpec as P

D = 2560


BETA_FIRST = 0.9
BETA_SECOND = 0.999
BIAS_FIRST = 0.9999734386011124
BIAS_SECOND = 0.0952078528862904
EPSILON = 1e-08
EPSILON_NORM = 1e-06
LEARNING_RATE = 0.1
GALORE_SCALE = 0.25


def adam_share(grad_share, first_moment, second_moment):
    first_next = BETA_FIRST * first_moment + (1.0 - BETA_FIRST) * grad_share
    second_next = BETA_SECOND * second_moment + (1.0 - BETA_SECOND) * grad_share * grad_share
    normal = first_next / BIAS_FIRST / (jnp.sqrt(second_next / BIAS_SECOND) + EPSILON)
    return (first_next, second_next, normal.astype(jnp.bfloat16))


def partner_perm(size, bit):
    return [(i, i ^ (1 << bit)) for i in range(size)]


def butterfly_sum(value, axis, size, bits=None):
    if bits is None:
        bits = range(size.bit_length() - 1)
    for bit in bits:
        value = value + lax.ppermute(value, axis, partner_perm(size, bit))
    return value


def halving_scatter(value, axis, size, stages):
    index = lax.axis_index(axis)
    for bit, dim in stages:
        half = value.shape[dim] // 2
        mine = (index >> bit) & 1
        keep = lax.dynamic_slice_in_dim(value, mine * half, half, dim)
        send = lax.dynamic_slice_in_dim(value, (1 - mine) * half, half, dim)
        value = keep + lax.ppermute(send, axis, partner_perm(size, bit))
    return value


def doubling_gather(value, axis, size, stages):
    index = lax.axis_index(axis)
    for bit, dim in reversed(stages):
        mine = (index >> bit) & 1
        other = lax.ppermute(value, axis, partner_perm(size, bit))
        low = jnp.where(mine == 0, value, other)
        high = jnp.where(mine == 0, other, value)
        value = jnp.concatenate([low, high], axis=dim)
    return value


def reverse_blocks(value, bits, width):
    lead = value.shape[:-1]
    split = value.reshape(lead + (2,) * bits + (width,))
    axes = tuple(range(len(lead))) + tuple(len(lead) + bits - 1 - i for i in range(bits)) + (len(lead) + bits,)
    return jnp.transpose(split, axes).reshape(value.shape)


def block_masks(shape):
    rows = lax.broadcasted_iota(jnp.int32, shape, 1)
    cols = lax.broadcasted_iota(jnp.int32, shape, 2)
    return rows < cols, rows == cols, rows > cols


def pack_gram(gram):
    h = gram.shape[1] // 2
    top_left, top_right, bottom_right = gram[:, :h, :h], gram[:, :h, h:], gram[:, h:, h:]
    upper, same, lower = block_masks(top_left.shape)
    folded = jnp.where(upper | same, top_left, bottom_right)
    corner = jnp.sum(jnp.where(same, bottom_right, 0.0), axis=1, keepdims=True)
    return jnp.concatenate([folded, top_right, corner], axis=1)


def unpack_gram(packed):
    h = packed.shape[2]
    folded, top_right, corner = packed[:, :h], packed[:, h : 2 * h], packed[:, 2 * h :]
    upper, same, lower = block_masks(folded.shape)
    flipped = jnp.transpose(folded, (0, 2, 1))
    top_left = jnp.where(upper | same, folded, flipped)
    bottom_right = jnp.where(lower, folded, jnp.where(same, corner, flipped))
    top = jnp.concatenate([top_left, top_right], axis=2)
    bottom = jnp.concatenate([jnp.transpose(top_right, (0, 2, 1)), bottom_right], axis=2)
    return jnp.concatenate([top, bottom], axis=1)


def shards(grads, weights, basis, first_moment, second_moment):
    highest = lax.Precision.HIGHEST
    fsdp = lax.axis_size("fsdp")
    tp = lax.axis_size("tp")
    width = first_moment.shape[2]
    rank_width = basis.shape[2]
    tp_bits = [(b, 2) for b in range(tp.bit_length() - 1)]
    basis_order = reverse_blocks(basis, len(tp_bits), width)

    projected_part = jnp.einsum("mfd,dmr->mfr", grads, basis_order, preferred_element_type=jnp.float32)
    own = halving_scatter(projected_part, "tp", tp, tp_bits)
    first_next, second_next, normal_half = adam_share(own, first_moment, second_moment)
    halves = jnp.stack([own.astype(jnp.bfloat16), normal_half], axis=0)
    gathered = doubling_gather(halves, "tp", tp, [(b, 3) for b, _ in tp_bits])
    projected_half, normal_full = gathered[0], gathered[1]

    image_part = jnp.einsum("mfd,mfr->mdr", grads, projected_half, preferred_element_type=jnp.float32)
    stages = [(0, 0), (1, 2), (3, 1)]
    chunk = halving_scatter(image_part, "fsdp", fsdp, stages)
    chunk = butterfly_sum(chunk, "fsdp", fsdp, [b for b in range(fsdp.bit_length() - 1) if b not in (0, 1, 3)])
    image = doubling_gather(chunk, "fsdp", fsdp, stages)

    update = jnp.einsum("mfr,dmr->mfd", normal_full, basis_order, preferred_element_type=jnp.float32)
    weight_next = weights - LEARNING_RATE * GALORE_SCALE * update

    gram = unpack_gram(butterfly_sum(pack_gram(jnp.einsum("mdr,mds->mrs", image, image, precision=highest)), "tp", tp))
    diagonal = lax.broadcasted_iota(jnp.int32, gram.shape, 1) == lax.broadcasted_iota(jnp.int32, gram.shape, 2)
    total = jnp.sum(jnp.where(diagonal, gram, 0.0), axis=(1, 2)) + EPSILON_NORM
    factor = jnp.sqrt(rank_width / total)
    scaled = image * factor[:, None, None]
    cross = gram * (factor * factor)[:, None, None]
    shaped = 1.5 * scaled - 0.5 * jnp.einsum("mdr,mrs->mds", scaled, cross, precision=highest)
    basis_next = reverse_blocks((jnp.sqrt(D / rank_width) * shaped).astype(jnp.bfloat16), len(tp_bits), width)
    return (weight_next, first_next, second_next, jnp.transpose(basis_next, (1, 0, 2)))


def solution(mesh):
    in_specs = (
        P(None, "fsdp", "tp"),
        P(None, "fsdp", "tp"),
        P("tp", None, None),
        P(None, "fsdp", "tp"),
        P(None, "fsdp", "tp"),
    )
    out_specs = (
        P(None, "fsdp", "tp"),
        P(None, "fsdp", "tp"),
        P(None, "fsdp", "tp"),
        P("tp", None, None),
    )
    return jax.shard_map(shards, mesh=mesh, in_specs=in_specs, out_specs=out_specs, check_vma=False)
```

```python
import jax
import jax.numpy as jnp
from jax import lax
from jax.sharding import PartitionSpec as P

D = 2560


BETA_FIRST = 0.9
BETA_SECOND = 0.999
BIAS_FIRST = 0.9999734386011124
BIAS_SECOND = 0.0952078528862904
EPSILON = 1e-08
EPSILON_NORM = 1e-06
LEARNING_RATE = 0.1
GALORE_SCALE = 0.25


def adam_share(grad_share, first_moment, second_moment):
    first_next = BETA_FIRST * first_moment + (1.0 - BETA_FIRST) * grad_share
    second_next = BETA_SECOND * second_moment + (1.0 - BETA_SECOND) * grad_share * grad_share
    normal = first_next / BIAS_FIRST / (jnp.sqrt(second_next / BIAS_SECOND) + EPSILON)
    return (first_next, second_next, normal.astype(jnp.bfloat16))


def partner_perm(size, bit):
    return [(i, i ^ (1 << bit)) for i in range(size)]


def butterfly_sum(value, axis, size, bits=None):
    if bits is None:
        bits = range(size.bit_length() - 1)
    for bit in bits:
        value = value + lax.ppermute(value, axis, partner_perm(size, bit))
    return value


def halving_scatter(value, axis, size, stages):
    index = lax.axis_index(axis)
    for bit, dim in stages:
        half = value.shape[dim] // 2
        mine = (index >> bit) & 1
        keep = lax.dynamic_slice_in_dim(value, mine * half, half, dim)
        send = lax.dynamic_slice_in_dim(value, (1 - mine) * half, half, dim)
        value = keep + lax.ppermute(send, axis, partner_perm(size, bit))
    return value


def doubling_gather(value, axis, size, stages):
    index = lax.axis_index(axis)
    for bit, dim in reversed(stages):
        mine = (index >> bit) & 1
        other = lax.ppermute(value, axis, partner_perm(size, bit))
        low = jnp.where(mine == 0, value, other)
        high = jnp.where(mine == 0, other, value)
        value = jnp.concatenate([low, high], axis=dim)
    return value


def reverse_blocks(value, bits, width):
    lead = value.shape[:-1]
    split = value.reshape(lead + (2,) * bits + (width,))
    axes = tuple(range(len(lead))) + tuple(len(lead) + bits - 1 - i for i in range(bits)) + (len(lead) + bits,)
    return jnp.transpose(split, axes).reshape(value.shape)


def block_masks(shape):
    rows = lax.broadcasted_iota(jnp.int32, shape, 1)
    cols = lax.broadcasted_iota(jnp.int32, shape, 2)
    return rows < cols, rows == cols, rows > cols


def pack_gram(gram):
    h = gram.shape[1] // 2
    top_left, top_right, bottom_right = gram[:, :h, :h], gram[:, :h, h:], gram[:, h:, h:]
    upper, same, lower = block_masks(top_left.shape)
    folded = jnp.where(upper | same, top_left, bottom_right)
    corner = jnp.sum(jnp.where(same, bottom_right, 0.0), axis=1, keepdims=True)
    return jnp.concatenate([folded, top_right, corner], axis=1)


def unpack_gram(packed):
    h = packed.shape[2]
    folded, top_right, corner = packed[:, :h], packed[:, h : 2 * h], packed[:, 2 * h :]
    upper, same, lower = block_masks(folded.shape)
    flipped = jnp.transpose(folded, (0, 2, 1))
    top_left = jnp.where(upper | same, folded, flipped)
    bottom_right = jnp.where(lower, folded, jnp.where(same, corner, flipped))
    top = jnp.concatenate([top_left, top_right], axis=2)
    bottom = jnp.concatenate([jnp.transpose(top_right, (0, 2, 1)), bottom_right], axis=2)
    return jnp.concatenate([top, bottom], axis=1)


def shards(grads, weights, basis, first_moment, second_moment):
    highest = lax.Precision.HIGHEST
    fsdp = lax.axis_size("fsdp")
    tp = lax.axis_size("tp")
    width = first_moment.shape[2]
    rank_width = basis.shape[2]
    tp_bits = [(b, 2) for b in range(tp.bit_length() - 1)]
    basis_order = reverse_blocks(basis, len(tp_bits), width)

    projected_part = jnp.einsum("mfd,dmr->mfr", grads, basis_order, preferred_element_type=jnp.float32)
    half = halving_scatter(projected_part, "tp", tp, [(0, 2)])
    moments = jnp.stack([first_moment, second_moment], axis=0)
    member = lax.axis_index("tp")
    own_place = 0
    for step, bit in enumerate(reversed(range(1, len(tp_bits)))):
        half_rows = half.size // 128
        message = jnp.concatenate([half.reshape(half_rows, 128), moments.reshape(-1, 128)], axis=0)
        arrived = lax.ppermute(message, "tp", partner_perm(tp, bit))
        half = half + arrived[:half_rows].reshape(half.shape)
        other = arrived[half_rows:].reshape(moments.shape)
        mine = (member >> bit) & 1
        moments = jnp.concatenate([jnp.where(mine == 0, moments, other), jnp.where(mine == 0, other, moments)], axis=3)
        own_place = own_place + (mine << step)
    first_half, second_half, normal_half = adam_share(half, moments[0], moments[1])
    first_next = lax.dynamic_slice_in_dim(first_half, own_place * width, width, 2)
    second_next = lax.dynamic_slice_in_dim(second_half, own_place * width, width, 2)
    halves = jnp.stack([half.astype(jnp.bfloat16), normal_half], axis=0)
    gathered = doubling_gather(halves, "tp", tp, [(0, 3)])
    projected_half, normal_full = gathered[0], gathered[1]

    image_part = jnp.einsum("mfd,mfr->mdr", grads, projected_half, preferred_element_type=jnp.float32)
    stages = [(0, 0), (1, 2), (3, 1)]
    chunk = halving_scatter(image_part, "fsdp", fsdp, stages)
    chunk = butterfly_sum(chunk, "fsdp", fsdp, [b for b in range(fsdp.bit_length() - 1) if b not in (0, 1, 3)])
    image = doubling_gather(chunk, "fsdp", fsdp, stages)

    update = jnp.einsum("mfr,dmr->mfd", normal_full, basis_order, preferred_element_type=jnp.float32)
    weight_next = weights - LEARNING_RATE * GALORE_SCALE * update

    gram = unpack_gram(butterfly_sum(pack_gram(jnp.einsum("mdr,mds->mrs", image, image, precision=highest)), "tp", tp))
    diagonal = lax.broadcasted_iota(jnp.int32, gram.shape, 1) == lax.broadcasted_iota(jnp.int32, gram.shape, 2)
    total = jnp.sum(jnp.where(diagonal, gram, 0.0), axis=(1, 2)) + EPSILON_NORM
    factor = jnp.sqrt(rank_width / total)
    scaled = image * factor[:, None, None]
    cross = gram * (factor * factor)[:, None, None]
    shaped = 1.5 * scaled - 0.5 * jnp.einsum("mdr,mrs->mds", scaled, cross, precision=highest)
    basis_next = reverse_blocks((jnp.sqrt(D / rank_width) * shaped).astype(jnp.bfloat16), len(tp_bits), width)
    return (weight_next, first_next, second_next, jnp.transpose(basis_next, (1, 0, 2)))


def solution(mesh):
    in_specs = (
        P(None, "fsdp", "tp"),
        P(None, "fsdp", "tp"),
        P("tp", None, None),
        P(None, "fsdp", "tp"),
        P(None, "fsdp", "tp"),
    )
    out_specs = (
        P(None, "fsdp", "tp"),
        P(None, "fsdp", "tp"),
        P(None, "fsdp", "tp"),
        P("tp", None, None),
    )
    return jax.shard_map(shards, mesh=mesh, in_specs=in_specs, out_specs=out_specs, check_vma=False)
```

```python
import jax
import jax.numpy as jnp
from jax import lax
from jax.sharding import PartitionSpec as P

D = 2560


BETA_FIRST = 0.9
BETA_SECOND = 0.999
BIAS_FIRST = 0.9999734386011124
BIAS_SECOND = 0.0952078528862904
EPSILON = 1e-08
EPSILON_NORM = 1e-06
LEARNING_RATE = 0.1
GALORE_SCALE = 0.25


def adam_share(grad_share, first_moment, second_moment):
    first_next = BETA_FIRST * first_moment + (1.0 - BETA_FIRST) * grad_share
    second_next = BETA_SECOND * second_moment + (1.0 - BETA_SECOND) * grad_share * grad_share
    normal = first_next / BIAS_FIRST / (jnp.sqrt(second_next / BIAS_SECOND) + EPSILON)
    return (first_next, second_next, normal.astype(jnp.bfloat16))


def partner_perm(size, bit):
    return [(i, i ^ (1 << bit)) for i in range(size)]


def butterfly_sum(value, axis, size, bits=None):
    if bits is None:
        bits = range(size.bit_length() - 1)
    for bit in bits:
        value = value + lax.ppermute(value, axis, partner_perm(size, bit))
    return value


def halving_scatter(value, axis, size, stages):
    index = lax.axis_index(axis)
    for bit, dim in stages:
        half = value.shape[dim] // 2
        mine = (index >> bit) & 1
        keep = lax.dynamic_slice_in_dim(value, mine * half, half, dim)
        send = lax.dynamic_slice_in_dim(value, (1 - mine) * half, half, dim)
        value = keep + lax.ppermute(send, axis, partner_perm(size, bit))
    return value


def doubling_gather(value, axis, size, stages):
    index = lax.axis_index(axis)
    for bit, dim in reversed(stages):
        mine = (index >> bit) & 1
        other = lax.ppermute(value, axis, partner_perm(size, bit))
        low = jnp.where(mine == 0, value, other)
        high = jnp.where(mine == 0, other, value)
        value = jnp.concatenate([low, high], axis=dim)
    return value


def reverse_blocks(value, bits, width):
    lead = value.shape[:-1]
    split = value.reshape(lead + (2,) * bits + (width,))
    axes = tuple(range(len(lead))) + tuple(len(lead) + bits - 1 - i for i in range(bits)) + (len(lead) + bits,)
    return jnp.transpose(split, axes).reshape(value.shape)


def block_masks(shape):
    rows = lax.broadcasted_iota(jnp.int32, shape, 1)
    cols = lax.broadcasted_iota(jnp.int32, shape, 2)
    return rows < cols, rows == cols, rows > cols


def pack_gram(gram):
    h = gram.shape[1] // 2
    top_left, top_right, bottom_right = gram[:, :h, :h], gram[:, :h, h:], gram[:, h:, h:]
    upper, same, lower = block_masks(top_left.shape)
    folded = jnp.where(upper | same, top_left, bottom_right)
    corner = jnp.sum(jnp.where(same, bottom_right, 0.0), axis=1, keepdims=True)
    return jnp.concatenate([folded, top_right, corner], axis=1)


def unpack_gram(packed):
    h = packed.shape[2]
    folded, top_right, corner = packed[:, :h], packed[:, h : 2 * h], packed[:, 2 * h :]
    upper, same, lower = block_masks(folded.shape)
    flipped = jnp.transpose(folded, (0, 2, 1))
    top_left = jnp.where(upper | same, folded, flipped)
    bottom_right = jnp.where(lower, folded, jnp.where(same, corner, flipped))
    top = jnp.concatenate([top_left, top_right], axis=2)
    bottom = jnp.concatenate([jnp.transpose(top_right, (0, 2, 1)), bottom_right], axis=2)
    return jnp.concatenate([top, bottom], axis=1)


def shards(grads, weights, basis, first_moment, second_moment):
    highest = lax.Precision.HIGHEST
    fsdp = lax.axis_size("fsdp")
    tp = lax.axis_size("tp")
    width = first_moment.shape[2]
    rank_width = basis.shape[2]
    tp_bits = [(b, 2) for b in range(tp.bit_length() - 1)]
    basis_order = reverse_blocks(basis, len(tp_bits), width)

    projected_part = jnp.einsum("mfd,dmr->mfr", grads, basis_order, preferred_element_type=jnp.float32)
    half = halving_scatter(projected_part, "tp", tp, [(0, 2)])
    moments = jnp.stack([first_moment, second_moment], axis=0)
    member = lax.axis_index("tp")
    own_place = 0
    for step, bit in enumerate(reversed(range(1, len(tp_bits)))):
        half_rows = half.size // 128
        message = jnp.concatenate([half.reshape(half_rows, 128), moments.reshape(-1, 128)], axis=0)
        arrived = lax.ppermute(message, "tp", partner_perm(tp, bit))
        half = half + arrived[:half_rows].reshape(half.shape)
        other = arrived[half_rows:].reshape(moments.shape)
        mine = (member >> bit) & 1
        moments = jnp.concatenate([jnp.where(mine == 0, moments, other), jnp.where(mine == 0, other, moments)], axis=3)
        own_place = own_place + (mine << step)
    first_half, second_half, normal_half = adam_share(half, moments[0], moments[1])
    first_next = lax.dynamic_slice_in_dim(first_half, own_place * width, width, 2)
    second_next = lax.dynamic_slice_in_dim(second_half, own_place * width, width, 2)
    halves = jnp.stack([half.astype(jnp.bfloat16), normal_half], axis=0)
    gathered = doubling_gather(halves, "tp", tp, [(0, 3)])
    projected_half, normal_full = gathered[0], gathered[1]

    image_part = jnp.einsum("mfd,mfr->mdr", grads, projected_half, preferred_element_type=jnp.float32)
    stages = [(0, 0), (1, 2), (3, 1)]
    chunk = halving_scatter(image_part, "fsdp", fsdp, stages)
    chunk = butterfly_sum(chunk, "fsdp", fsdp, [b for b in range(fsdp.bit_length() - 1) if b not in (0, 1, 3)])
    image = doubling_gather(chunk, "fsdp", fsdp, stages)

    update = jnp.einsum("mfr,dmr->mfd", normal_full, basis_order, preferred_element_type=jnp.float32)
    weight_next = weights - LEARNING_RATE * GALORE_SCALE * update

    packed = halving_scatter(pack_gram(jnp.einsum("mdr,mds->mrs", image, image, precision=highest)), "tp", tp, [(0, 0)])
    packed = butterfly_sum(packed, "tp", tp, range(1, len(tp_bits)))
    gram = unpack_gram(doubling_gather(packed, "tp", tp, [(0, 0)]))
    diagonal = lax.broadcasted_iota(jnp.int32, gram.shape, 1) == lax.broadcasted_iota(jnp.int32, gram.shape, 2)
    total = jnp.sum(jnp.where(diagonal, gram, 0.0), axis=(1, 2)) + EPSILON_NORM
    factor = jnp.sqrt(rank_width / total)
    scaled = image * factor[:, None, None]
    cross = gram * (factor * factor)[:, None, None]
    shaped = 1.5 * scaled - 0.5 * jnp.einsum("mdr,mrs->mds", scaled, cross, precision=highest)
    basis_next = reverse_blocks((jnp.sqrt(D / rank_width) * shaped).astype(jnp.bfloat16), len(tp_bits), width)
    return (weight_next, first_next, second_next, jnp.transpose(basis_next, (1, 0, 2)))


def solution(mesh):
    in_specs = (
        P(None, "fsdp", "tp"),
        P(None, "fsdp", "tp"),
        P("tp", None, None),
        P(None, "fsdp", "tp"),
        P(None, "fsdp", "tp"),
    )
    out_specs = (
        P(None, "fsdp", "tp"),
        P(None, "fsdp", "tp"),
        P(None, "fsdp", "tp"),
        P("tp", None, None),
    )
    return jax.shard_map(shards, mesh=mesh, in_specs=in_specs, out_specs=out_specs, check_vma=False)
```

```python
import jax
import jax.numpy as jnp
from jax import lax
from jax.sharding import PartitionSpec as P

D = 2560


BETA_FIRST = 0.9
BETA_SECOND = 0.999
BIAS_FIRST = 0.9999734386011124
BIAS_SECOND = 0.0952078528862904
EPSILON = 1e-08
EPSILON_NORM = 1e-06
LEARNING_RATE = 0.1
GALORE_SCALE = 0.25


def adam_share(grad_share, first_moment, second_moment):
    first_next = BETA_FIRST * first_moment + (1.0 - BETA_FIRST) * grad_share
    second_next = BETA_SECOND * second_moment + (1.0 - BETA_SECOND) * grad_share * grad_share
    normal = first_next / BIAS_FIRST / (jnp.sqrt(second_next / BIAS_SECOND) + EPSILON)
    return (first_next, second_next, normal.astype(jnp.bfloat16))


def partner_perm(size, bit):
    return [(i, i ^ (1 << bit)) for i in range(size)]


def butterfly_sum(value, axis, size, bits=None):
    if bits is None:
        bits = range(size.bit_length() - 1)
    for bit in bits:
        value = value + lax.ppermute(value, axis, partner_perm(size, bit))
    return value


def halving_scatter(value, axis, size, stages):
    index = lax.axis_index(axis)
    for bit, dim in stages:
        half = value.shape[dim] // 2
        mine = (index >> bit) & 1
        keep = lax.dynamic_slice_in_dim(value, mine * half, half, dim)
        send = lax.dynamic_slice_in_dim(value, (1 - mine) * half, half, dim)
        value = keep + lax.ppermute(send, axis, partner_perm(size, bit))
    return value


def doubling_gather(value, axis, size, stages):
    index = lax.axis_index(axis)
    for bit, dim in reversed(stages):
        mine = (index >> bit) & 1
        other = lax.ppermute(value, axis, partner_perm(size, bit))
        low = jnp.where(mine == 0, value, other)
        high = jnp.where(mine == 0, other, value)
        value = jnp.concatenate([low, high], axis=dim)
    return value


def reverse_blocks(value, bits, width):
    lead = value.shape[:-1]
    split = value.reshape(lead + (2,) * bits + (width,))
    axes = tuple(range(len(lead))) + tuple(len(lead) + bits - 1 - i for i in range(bits)) + (len(lead) + bits,)
    return jnp.transpose(split, axes).reshape(value.shape)


def block_masks(shape):
    rows = lax.broadcasted_iota(jnp.int32, shape, 1)
    cols = lax.broadcasted_iota(jnp.int32, shape, 2)
    return rows < cols, rows == cols, rows > cols


def pack_gram(gram):
    h = gram.shape[1] // 2
    top_left, top_right, bottom_right = gram[:, :h, :h], gram[:, :h, h:], gram[:, h:, h:]
    upper, same, lower = block_masks(top_left.shape)
    folded = jnp.where(upper | same, top_left, bottom_right)
    corner = jnp.sum(jnp.where(same, bottom_right, 0.0), axis=1, keepdims=True)
    return jnp.concatenate([folded, top_right, corner], axis=1)


def unpack_gram(packed):
    h = packed.shape[2]
    folded, top_right, corner = packed[:, :h], packed[:, h : 2 * h], packed[:, 2 * h :]
    upper, same, lower = block_masks(folded.shape)
    flipped = jnp.transpose(folded, (0, 2, 1))
    top_left = jnp.where(upper | same, folded, flipped)
    bottom_right = jnp.where(lower, folded, jnp.where(same, corner, flipped))
    top = jnp.concatenate([top_left, top_right], axis=2)
    bottom = jnp.concatenate([jnp.transpose(top_right, (0, 2, 1)), bottom_right], axis=2)
    return jnp.concatenate([top, bottom], axis=1)


def shards(grads, weights, basis, first_moment, second_moment):
    highest = lax.Precision.HIGHEST
    fsdp = lax.axis_size("fsdp")
    tp = lax.axis_size("tp")
    width = first_moment.shape[2]
    rank_width = basis.shape[2]
    tp_bits = [(b, 2) for b in range(tp.bit_length() - 1)]
    basis_order = reverse_blocks(basis, len(tp_bits), width)

    projected_part = jnp.einsum("mfd,dmr->mfr", grads, basis_order, preferred_element_type=jnp.float32)
    half = halving_scatter(projected_part, "tp", tp, [(0, 2)])
    half = butterfly_sum(half, "tp", tp, reversed(range(1, len(tp_bits))))
    member = lax.axis_index("tp")
    own_place = 0
    for step, bit in enumerate(reversed(range(1, len(tp_bits)))):
        own_place = own_place + (((member >> bit) & 1) << step)
    own = lax.dynamic_slice_in_dim(half, own_place * width, width, 2)
    first_next, second_next, normal_half = adam_share(own, first_moment, second_moment)
    projected_half = doubling_gather(half.astype(jnp.bfloat16), "tp", tp, [(0, 2)])
    normal_full = doubling_gather(normal_half, "tp", tp, tp_bits)

    image_part = jnp.einsum("mfd,mfr->mdr", grads, projected_half, preferred_element_type=jnp.float32)
    stages = [(0, 0), (1, 2), (3, 1)]
    chunk = halving_scatter(image_part, "fsdp", fsdp, stages)
    chunk = butterfly_sum(chunk, "fsdp", fsdp, [b for b in range(fsdp.bit_length() - 1) if b not in (0, 1, 3)])
    image = doubling_gather(chunk, "fsdp", fsdp, stages)

    update = jnp.einsum("mfr,dmr->mfd", normal_full, basis_order, preferred_element_type=jnp.float32)
    weight_next = weights - LEARNING_RATE * GALORE_SCALE * update

    packed = halving_scatter(pack_gram(jnp.einsum("mdr,mds->mrs", image, image, precision=highest)), "tp", tp, [(0, 0)])
    packed = butterfly_sum(packed, "tp", tp, range(1, len(tp_bits)))
    gram = unpack_gram(doubling_gather(packed, "tp", tp, [(0, 0)]))
    diagonal = lax.broadcasted_iota(jnp.int32, gram.shape, 1) == lax.broadcasted_iota(jnp.int32, gram.shape, 2)
    total = jnp.sum(jnp.where(diagonal, gram, 0.0), axis=(1, 2)) + EPSILON_NORM
    factor = jnp.sqrt(rank_width / total)
    scaled = image * factor[:, None, None]
    cross = gram * (factor * factor)[:, None, None]
    shaped = 1.5 * scaled - 0.5 * jnp.einsum("mdr,mrs->mds", scaled, cross, precision=highest)
    basis_next = reverse_blocks((jnp.sqrt(D / rank_width) * shaped).astype(jnp.bfloat16), len(tp_bits), width)
    return (weight_next, first_next, second_next, jnp.transpose(basis_next, (1, 0, 2)))


def solution(mesh):
    in_specs = (
        P(None, "fsdp", "tp"),
        P(None, "fsdp", "tp"),
        P("tp", None, None),
        P(None, "fsdp", "tp"),
        P(None, "fsdp", "tp"),
    )
    out_specs = (
        P(None, "fsdp", "tp"),
        P(None, "fsdp", "tp"),
        P(None, "fsdp", "tp"),
        P("tp", None, None),
    )
    return jax.shard_map(shards, mesh=mesh, in_specs=in_specs, out_specs=out_specs, check_vma=False)
```

```python
import jax
import jax.numpy as jnp
from jax import lax
from jax.sharding import PartitionSpec as P

D = 2560


BETA_FIRST = 0.9
BETA_SECOND = 0.999
BIAS_FIRST = 0.9999734386011124
BIAS_SECOND = 0.0952078528862904
EPSILON = 1e-08
EPSILON_NORM = 1e-06
LEARNING_RATE = 0.1
GALORE_SCALE = 0.25


def adam_share(grad_share, first_moment, second_moment):
    first_next = BETA_FIRST * first_moment + (1.0 - BETA_FIRST) * grad_share
    second_next = BETA_SECOND * second_moment + (1.0 - BETA_SECOND) * grad_share * grad_share
    normal = first_next / BIAS_FIRST / (jnp.sqrt(second_next / BIAS_SECOND) + EPSILON)
    return (first_next, second_next, normal.astype(jnp.bfloat16))


def partner_perm(size, bit):
    return [(i, i ^ (1 << bit)) for i in range(size)]


def butterfly_sum(value, axis, size, bits=None):
    if bits is None:
        bits = range(size.bit_length() - 1)
    for bit in bits:
        value = value + lax.ppermute(value, axis, partner_perm(size, bit))
    return value


def halving_scatter(value, axis, size, stages):
    index = lax.axis_index(axis)
    for bit, dim in stages:
        half = value.shape[dim] // 2
        mine = (index >> bit) & 1
        keep = lax.dynamic_slice_in_dim(value, mine * half, half, dim)
        send = lax.dynamic_slice_in_dim(value, (1 - mine) * half, half, dim)
        value = keep + lax.ppermute(send, axis, partner_perm(size, bit))
    return value


def doubling_gather(value, axis, size, stages):
    index = lax.axis_index(axis)
    for bit, dim in reversed(stages):
        mine = (index >> bit) & 1
        other = lax.ppermute(value, axis, partner_perm(size, bit))
        low = jnp.where(mine == 0, value, other)
        high = jnp.where(mine == 0, other, value)
        value = jnp.concatenate([low, high], axis=dim)
    return value


def reverse_blocks(value, bits, width):
    lead = value.shape[:-1]
    split = value.reshape(lead + (2,) * bits + (width,))
    axes = tuple(range(len(lead))) + tuple(len(lead) + bits - 1 - i for i in range(bits)) + (len(lead) + bits,)
    return jnp.transpose(split, axes).reshape(value.shape)


def block_masks(shape):
    rows = lax.broadcasted_iota(jnp.int32, shape, 1)
    cols = lax.broadcasted_iota(jnp.int32, shape, 2)
    return rows < cols, rows == cols, rows > cols


def pack_gram(gram):
    h = gram.shape[1] // 2
    top_left, top_right, bottom_right = gram[:, :h, :h], gram[:, :h, h:], gram[:, h:, h:]
    upper, same, lower = block_masks(top_left.shape)
    folded = jnp.where(upper | same, top_left, bottom_right)
    corner = jnp.sum(jnp.where(same, bottom_right, 0.0), axis=1, keepdims=True)
    return jnp.concatenate([folded, top_right, corner], axis=1)


def unpack_gram(packed):
    h = packed.shape[2]
    folded, top_right, corner = packed[:, :h], packed[:, h : 2 * h], packed[:, 2 * h :]
    upper, same, lower = block_masks(folded.shape)
    flipped = jnp.transpose(folded, (0, 2, 1))
    top_left = jnp.where(upper | same, folded, flipped)
    bottom_right = jnp.where(lower, folded, jnp.where(same, corner, flipped))
    top = jnp.concatenate([top_left, top_right], axis=2)
    bottom = jnp.concatenate([jnp.transpose(top_right, (0, 2, 1)), bottom_right], axis=2)
    return jnp.concatenate([top, bottom], axis=1)


def shards(grads, weights, basis, first_moment, second_moment):
    highest = lax.Precision.HIGHEST
    fsdp = lax.axis_size("fsdp")
    tp = lax.axis_size("tp")
    width = first_moment.shape[2]
    rank_width = basis.shape[2]
    tp_bits = [(b, 2) for b in range(tp.bit_length() - 1)]
    basis_order = reverse_blocks(basis, len(tp_bits), width)

    projected_part = jnp.einsum("mfd,dmr->mfr", grads, basis_order, preferred_element_type=jnp.float32)
    half = halving_scatter(projected_part, "tp", tp, [(0, 2)])
    half = butterfly_sum(half, "tp", tp, reversed(range(1, len(tp_bits))))
    member = lax.axis_index("tp")
    own_place = 0
    for step, bit in enumerate(reversed(range(1, len(tp_bits)))):
        own_place = own_place + (((member >> bit) & 1) << step)
    own = lax.dynamic_slice_in_dim(half, own_place * width, width, 2)
    first_next, second_next, normal_half = adam_share(own, first_moment, second_moment)
    projected_half = doubling_gather(half.astype(jnp.bfloat16), "tp", tp, [(0, 2)])
    normal_full = doubling_gather(normal_half, "tp", tp, tp_bits)

    image_part = jnp.einsum("mfd,mfr->mdr", grads, projected_half, preferred_element_type=jnp.float32)
    stages = [(0, 0), (1, 2), (3, 1)]
    chunk = halving_scatter(image_part, "fsdp", fsdp, stages)
    chunk = butterfly_sum(chunk, "fsdp", fsdp, [b for b in range(fsdp.bit_length() - 1) if b not in (0, 1, 3)])
    image = doubling_gather(chunk, "fsdp", fsdp, stages[1:])

    update = jnp.einsum("mfr,dmr->mfd", normal_full, basis_order, preferred_element_type=jnp.float32)
    weight_next = weights - LEARNING_RATE * GALORE_SCALE * update

    packed = pack_gram(jnp.einsum("mdr,mds->mrs", image, image, precision=highest))
    gram = unpack_gram(butterfly_sum(packed, "tp", tp))
    diagonal = lax.broadcasted_iota(jnp.int32, gram.shape, 1) == lax.broadcasted_iota(jnp.int32, gram.shape, 2)
    total = jnp.sum(jnp.where(diagonal, gram, 0.0), axis=(1, 2)) + EPSILON_NORM
    factor = jnp.sqrt(rank_width / total)
    scaled = image * factor[:, None, None]
    cross = gram * (factor * factor)[:, None, None]
    shaped = 1.5 * scaled - 0.5 * jnp.einsum("mdr,mrs->mds", scaled, cross, precision=highest)
    basis_own = (jnp.sqrt(D / rank_width) * shaped).astype(jnp.bfloat16)
    basis_next = reverse_blocks(doubling_gather(basis_own, "fsdp", fsdp, stages[:1]), len(tp_bits), width)
    return (weight_next, first_next, second_next, jnp.transpose(basis_next, (1, 0, 2)))


def solution(mesh):
    in_specs = (
        P(None, "fsdp", "tp"),
        P(None, "fsdp", "tp"),
        P("tp", None, None),
        P(None, "fsdp", "tp"),
        P(None, "fsdp", "tp"),
    )
    out_specs = (
        P(None, "fsdp", "tp"),
        P(None, "fsdp", "tp"),
        P(None, "fsdp", "tp"),
        P("tp", None, None),
    )
    return jax.shard_map(shards, mesh=mesh, in_specs=in_specs, out_specs=out_specs, check_vma=False)
```

```python
import jax
import jax.numpy as jnp
from jax import lax
from jax.sharding import PartitionSpec as P

D = 2560


BETA_FIRST = 0.9
BETA_SECOND = 0.999
BIAS_FIRST = 0.9999734386011124
BIAS_SECOND = 0.0952078528862904
EPSILON = 1e-08
EPSILON_NORM = 1e-06
LEARNING_RATE = 0.1
GALORE_SCALE = 0.25


def adam_share(grad_share, first_moment, second_moment):
    first_next = BETA_FIRST * first_moment + (1.0 - BETA_FIRST) * grad_share
    second_next = BETA_SECOND * second_moment + (1.0 - BETA_SECOND) * grad_share * grad_share
    normal = first_next / BIAS_FIRST / (jnp.sqrt(second_next / BIAS_SECOND) + EPSILON)
    return (first_next, second_next, normal.astype(jnp.bfloat16))


def partner_perm(size, bit):
    return [(i, i ^ (1 << bit)) for i in range(size)]


def butterfly_sum(value, axis, size, bits=None):
    if bits is None:
        bits = range(size.bit_length() - 1)
    for bit in bits:
        value = value + lax.ppermute(value, axis, partner_perm(size, bit))
    return value


def halving_scatter(value, axis, size, stages):
    index = lax.axis_index(axis)
    for bit, dim in stages:
        half = value.shape[dim] // 2
        mine = (index >> bit) & 1
        keep = lax.dynamic_slice_in_dim(value, mine * half, half, dim)
        send = lax.dynamic_slice_in_dim(value, (1 - mine) * half, half, dim)
        value = keep + lax.ppermute(send, axis, partner_perm(size, bit))
    return value


def doubling_gather(value, axis, size, stages):
    index = lax.axis_index(axis)
    for bit, dim in reversed(stages):
        mine = (index >> bit) & 1
        other = lax.ppermute(value, axis, partner_perm(size, bit))
        low = jnp.where(mine == 0, value, other)
        high = jnp.where(mine == 0, other, value)
        value = jnp.concatenate([low, high], axis=dim)
    return value


def reverse_blocks(value, bits, width):
    lead = value.shape[:-1]
    split = value.reshape(lead + (2,) * bits + (width,))
    axes = tuple(range(len(lead))) + tuple(len(lead) + bits - 1 - i for i in range(bits)) + (len(lead) + bits,)
    return jnp.transpose(split, axes).reshape(value.shape)


def block_masks(shape):
    rows = lax.broadcasted_iota(jnp.int32, shape, 1)
    cols = lax.broadcasted_iota(jnp.int32, shape, 2)
    return rows < cols, rows == cols, rows > cols


def pack_gram(gram):
    h = gram.shape[1] // 2
    top_left, top_right, bottom_right = gram[:, :h, :h], gram[:, :h, h:], gram[:, h:, h:]
    upper, same, lower = block_masks(top_left.shape)
    folded = jnp.where(upper | same, top_left, bottom_right)
    corner = jnp.sum(jnp.where(same, bottom_right, 0.0), axis=1, keepdims=True)
    return jnp.concatenate([folded, top_right, corner], axis=1)


def unpack_gram(packed):
    h = packed.shape[2]
    folded, top_right, corner = packed[:, :h], packed[:, h : 2 * h], packed[:, 2 * h :]
    upper, same, lower = block_masks(folded.shape)
    flipped = jnp.transpose(folded, (0, 2, 1))
    top_left = jnp.where(upper | same, folded, flipped)
    bottom_right = jnp.where(lower, folded, jnp.where(same, corner, flipped))
    top = jnp.concatenate([top_left, top_right], axis=2)
    bottom = jnp.concatenate([jnp.transpose(top_right, (0, 2, 1)), bottom_right], axis=2)
    return jnp.concatenate([top, bottom], axis=1)


def shards(grads, weights, basis, first_moment, second_moment):
    highest = lax.Precision.HIGHEST
    fsdp = lax.axis_size("fsdp")
    tp = lax.axis_size("tp")
    width = first_moment.shape[2]
    rank_width = basis.shape[2]
    tp_bits = [(b, 2) for b in range(tp.bit_length() - 1)]
    basis_order = reverse_blocks(basis, len(tp_bits), width)

    projected_part = jnp.einsum("mfd,dmr->mfr", grads, basis_order, preferred_element_type=jnp.float32)
    last = len(tp_bits) - 1
    quarter = halving_scatter(projected_part, "tp", tp, tp_bits[:last])
    moments = jnp.stack([first_moment, second_moment], axis=0)
    rows = quarter.size // 128
    message = jnp.concatenate([quarter.reshape(rows, 128), moments.reshape(-1, 128)], axis=0)
    arrived = lax.ppermute(message, "tp", partner_perm(tp, last))
    quarter = quarter + arrived[:rows].reshape(quarter.shape)
    other = arrived[rows:].reshape(moments.shape)
    mine = (lax.axis_index("tp") >> last) & 1
    moments = jnp.concatenate([jnp.where(mine == 0, moments, other), jnp.where(mine == 0, other, moments)], axis=3)
    first_pair, second_pair, normal_pair = adam_share(quarter, moments[0], moments[1])
    first_next = lax.dynamic_slice_in_dim(first_pair, mine * width, width, 2)
    second_next = lax.dynamic_slice_in_dim(second_pair, mine * width, width, 2)
    halves = jnp.stack([quarter.astype(jnp.bfloat16), normal_pair], axis=0)
    gathered = doubling_gather(halves, "tp", tp, [(b, 3) for b, _ in tp_bits[:last]])
    projected_half, normal_full = gathered[0], gathered[1]

    image_part = jnp.einsum("mfd,mfr->mdr", grads, projected_half, preferred_element_type=jnp.float32)
    stages = [(0, 0), (1, 2), (3, 1)]
    chunk = halving_scatter(image_part, "fsdp", fsdp, stages)
    chunk = butterfly_sum(chunk, "fsdp", fsdp, [b for b in range(fsdp.bit_length() - 1) if b not in (0, 1, 3)])
    image = doubling_gather(chunk, "fsdp", fsdp, stages[1:])

    update = jnp.einsum("mfr,dmr->mfd", normal_full, basis_order, preferred_element_type=jnp.float32)
    weight_next = weights - LEARNING_RATE * GALORE_SCALE * update

    packed = pack_gram(jnp.einsum("mdr,mds->mrs", image, image, precision=highest))
    gram = unpack_gram(butterfly_sum(packed, "tp", tp))
    diagonal = lax.broadcasted_iota(jnp.int32, gram.shape, 1) == lax.broadcasted_iota(jnp.int32, gram.shape, 2)
    total = jnp.sum(jnp.where(diagonal, gram, 0.0), axis=(1, 2)) + EPSILON_NORM
    factor = jnp.sqrt(rank_width / total)
    scaled = image * factor[:, None, None]
    cross = gram * (factor * factor)[:, None, None]
    shaped = 1.5 * scaled - 0.5 * jnp.einsum("mdr,mrs->mds", scaled, cross, precision=highest)
    basis_own = (jnp.sqrt(D / rank_width) * shaped).astype(jnp.bfloat16)
    basis_next = reverse_blocks(doubling_gather(basis_own, "fsdp", fsdp, stages[:1]), len(tp_bits), width)
    return (weight_next, first_next, second_next, jnp.transpose(basis_next, (1, 0, 2)))


def solution(mesh):
    in_specs = (
        P(None, "fsdp", "tp"),
        P(None, "fsdp", "tp"),
        P("tp", None, None),
        P(None, "fsdp", "tp"),
        P(None, "fsdp", "tp"),
    )
    out_specs = (
        P(None, "fsdp", "tp"),
        P(None, "fsdp", "tp"),
        P(None, "fsdp", "tp"),
        P("tp", None, None),
    )
    return jax.shard_map(shards, mesh=mesh, in_specs=in_specs, out_specs=out_specs, check_vma=False)
```

```python
import jax
import jax.numpy as jnp
from jax import lax
from jax.sharding import PartitionSpec as P

D = 2560


BETA_FIRST = 0.9
BETA_SECOND = 0.999
BIAS_FIRST = 0.9999734386011124
BIAS_SECOND = 0.0952078528862904
EPSILON = 1e-08
EPSILON_NORM = 1e-06
LEARNING_RATE = 0.1
GALORE_SCALE = 0.25


def adam_share(grad_share, first_moment, second_moment):
    first_next = BETA_FIRST * first_moment + (1.0 - BETA_FIRST) * grad_share
    second_next = BETA_SECOND * second_moment + (1.0 - BETA_SECOND) * grad_share * grad_share
    normal = first_next / BIAS_FIRST / (jnp.sqrt(second_next / BIAS_SECOND) + EPSILON)
    return (first_next, second_next, normal.astype(jnp.bfloat16))


def partner_perm(size, bit):
    return [(i, i ^ (1 << bit)) for i in range(size)]


def butterfly_sum(value, axis, size, bits=None):
    if bits is None:
        bits = range(size.bit_length() - 1)
    for bit in bits:
        value = value + lax.ppermute(value, axis, partner_perm(size, bit))
    return value


def halving_scatter(value, axis, size, stages):
    index = lax.axis_index(axis)
    for bit, dim in stages:
        half = value.shape[dim] // 2
        mine = (index >> bit) & 1
        keep = lax.dynamic_slice_in_dim(value, mine * half, half, dim)
        send = lax.dynamic_slice_in_dim(value, (1 - mine) * half, half, dim)
        value = keep + lax.ppermute(send, axis, partner_perm(size, bit))
    return value


def doubling_gather(value, axis, size, stages):
    index = lax.axis_index(axis)
    for bit, dim in reversed(stages):
        mine = (index >> bit) & 1
        other = lax.ppermute(value, axis, partner_perm(size, bit))
        low = jnp.where(mine == 0, value, other)
        high = jnp.where(mine == 0, other, value)
        value = jnp.concatenate([low, high], axis=dim)
    return value


def reverse_blocks(value, bits, width):
    lead = value.shape[:-1]
    split = value.reshape(lead + (2,) * bits + (width,))
    axes = tuple(range(len(lead))) + tuple(len(lead) + bits - 1 - i for i in range(bits)) + (len(lead) + bits,)
    return jnp.transpose(split, axes).reshape(value.shape)


def block_masks(shape):
    rows = lax.broadcasted_iota(jnp.int32, shape, 1)
    cols = lax.broadcasted_iota(jnp.int32, shape, 2)
    return rows < cols, rows == cols, rows > cols


def pack_gram(gram):
    h = gram.shape[1] // 2
    top_left, top_right, bottom_right = gram[:, :h, :h], gram[:, :h, h:], gram[:, h:, h:]
    upper, same, lower = block_masks(top_left.shape)
    folded = jnp.where(upper | same, top_left, bottom_right)
    corner = jnp.sum(jnp.where(same, bottom_right, 0.0), axis=1, keepdims=True)
    return jnp.concatenate([folded, top_right, corner], axis=1)


def unpack_gram(packed):
    h = packed.shape[2]
    folded, top_right, corner = packed[:, :h], packed[:, h : 2 * h], packed[:, 2 * h :]
    upper, same, lower = block_masks(folded.shape)
    flipped = jnp.transpose(folded, (0, 2, 1))
    top_left = jnp.where(upper | same, folded, flipped)
    bottom_right = jnp.where(lower, folded, jnp.where(same, corner, flipped))
    top = jnp.concatenate([top_left, top_right], axis=2)
    bottom = jnp.concatenate([jnp.transpose(top_right, (0, 2, 1)), bottom_right], axis=2)
    return jnp.concatenate([top, bottom], axis=1)


def shards(grads, weights, basis, first_moment, second_moment):
    highest = lax.Precision.HIGHEST
    fsdp = lax.axis_size("fsdp")
    tp = lax.axis_size("tp")
    width = first_moment.shape[2]
    rank_width = basis.shape[2]
    tp_bits = [(b, 2) for b in range(tp.bit_length() - 1)]
    basis_order = reverse_blocks(basis, len(tp_bits), width)

    projected_part = jnp.einsum("mfd,dmr->mfr", grads, basis_order, preferred_element_type=jnp.float32)
    half = halving_scatter(projected_part, "tp", tp, [(0, 2)])
    half = butterfly_sum(half, "tp", tp, reversed(range(1, len(tp_bits))))
    member = lax.axis_index("tp")
    own_place = 0
    for step, bit in enumerate(reversed(range(1, len(tp_bits)))):
        own_place = own_place + (((member >> bit) & 1) << step)
    own = lax.dynamic_slice_in_dim(half, own_place * width, width, 2)
    first_next, second_next, normal_half = adam_share(own, first_moment, second_moment)
    projected_half = doubling_gather(half.astype(jnp.bfloat16), "tp", tp, [(0, 2)])
    normal_full = doubling_gather(normal_half, "tp", tp, list(reversed(tp_bits)))

    image_part = jnp.einsum("mfd,mfr->mdr", grads, projected_half, preferred_element_type=jnp.float32)
    stages = [(0, 0), (1, 2), (3, 1)]
    chunk = halving_scatter(image_part, "fsdp", fsdp, stages)
    chunk = butterfly_sum(chunk, "fsdp", fsdp, [b for b in range(fsdp.bit_length() - 1) if b not in (0, 1, 3)])
    image = doubling_gather(chunk, "fsdp", fsdp, stages[1:])

    update = jnp.einsum("mfr,dmr->mfd", normal_full, basis, preferred_element_type=jnp.float32)
    weight_next = weights - LEARNING_RATE * GALORE_SCALE * update

    packed = pack_gram(jnp.einsum("mdr,mds->mrs", image, image, precision=highest))
    gram = unpack_gram(butterfly_sum(packed, "tp", tp))
    diagonal = lax.broadcasted_iota(jnp.int32, gram.shape, 1) == lax.broadcasted_iota(jnp.int32, gram.shape, 2)
    total = jnp.sum(jnp.where(diagonal, gram, 0.0), axis=(1, 2)) + EPSILON_NORM
    factor = jnp.sqrt(rank_width / total)
    scaled = image * factor[:, None, None]
    cross = gram * (factor * factor)[:, None, None]
    shaped = 1.5 * scaled - 0.5 * jnp.einsum("mdr,mrs->mds", scaled, cross, precision=highest)
    basis_own = (jnp.sqrt(D / rank_width) * shaped).astype(jnp.bfloat16)
    basis_next = reverse_blocks(doubling_gather(basis_own, "fsdp", fsdp, stages[:1]), len(tp_bits), width)
    return (weight_next, first_next, second_next, jnp.transpose(basis_next, (1, 0, 2)))


def solution(mesh):
    in_specs = (
        P(None, "fsdp", "tp"),
        P(None, "fsdp", "tp"),
        P("tp", None, None),
        P(None, "fsdp", "tp"),
        P(None, "fsdp", "tp"),
    )
    out_specs = (
        P(None, "fsdp", "tp"),
        P(None, "fsdp", "tp"),
        P(None, "fsdp", "tp"),
        P("tp", None, None),
    )
    return jax.shard_map(shards, mesh=mesh, in_specs=in_specs, out_specs=out_specs, check_vma=False)
```

```python
import jax
import jax.numpy as jnp
from jax import lax
from jax.sharding import PartitionSpec as P

D = 2560


BETA_FIRST = 0.9
BETA_SECOND = 0.999
BIAS_FIRST = 0.9999734386011124
BIAS_SECOND = 0.0952078528862904
EPSILON = 1e-08
EPSILON_NORM = 1e-06
LEARNING_RATE = 0.1
GALORE_SCALE = 0.25


def adam_share(grad_share, first_moment, second_moment):
    first_next = BETA_FIRST * first_moment + (1.0 - BETA_FIRST) * grad_share
    second_next = BETA_SECOND * second_moment + (1.0 - BETA_SECOND) * grad_share * grad_share
    normal = first_next / BIAS_FIRST / (jnp.sqrt(second_next / BIAS_SECOND) + EPSILON)
    return (first_next, second_next, normal.astype(jnp.bfloat16))


def partner_perm(size, bit):
    return [(i, i ^ (1 << bit)) for i in range(size)]


def butterfly_sum(value, axis, size, bits=None):
    if bits is None:
        bits = range(size.bit_length() - 1)
    for bit in bits:
        value = value + lax.ppermute(value, axis, partner_perm(size, bit))
    return value


def halving_scatter(value, axis, size, stages):
    index = lax.axis_index(axis)
    for bit, dim in stages:
        half = value.shape[dim] // 2
        mine = (index >> bit) & 1
        keep = lax.dynamic_slice_in_dim(value, mine * half, half, dim)
        send = lax.dynamic_slice_in_dim(value, (1 - mine) * half, half, dim)
        value = keep + lax.ppermute(send, axis, partner_perm(size, bit))
    return value


def doubling_gather(value, axis, size, stages):
    index = lax.axis_index(axis)
    for bit, dim in reversed(stages):
        mine = (index >> bit) & 1
        other = lax.ppermute(value, axis, partner_perm(size, bit))
        low = jnp.where(mine == 0, value, other)
        high = jnp.where(mine == 0, other, value)
        value = jnp.concatenate([low, high], axis=dim)
    return value


def reverse_blocks(value, bits, width):
    lead = value.shape[:-1]
    split = value.reshape(lead + (2,) * bits + (width,))
    axes = tuple(range(len(lead))) + tuple(len(lead) + bits - 1 - i for i in range(bits)) + (len(lead) + bits,)
    return jnp.transpose(split, axes).reshape(value.shape)


def block_masks(shape):
    rows = lax.broadcasted_iota(jnp.int32, shape, 1)
    cols = lax.broadcasted_iota(jnp.int32, shape, 2)
    return rows < cols, rows == cols, rows > cols


def pack_gram(gram):
    h = gram.shape[1] // 2
    top_left, top_right, bottom_right = gram[:, :h, :h], gram[:, :h, h:], gram[:, h:, h:]
    upper, same, lower = block_masks(top_left.shape)
    folded = jnp.where(upper | same, top_left, bottom_right)
    corner = jnp.sum(jnp.where(same, bottom_right, 0.0), axis=1, keepdims=True)
    return jnp.concatenate([folded, top_right, corner], axis=1)


def unpack_gram(packed):
    h = packed.shape[2]
    folded, top_right, corner = packed[:, :h], packed[:, h : 2 * h], packed[:, 2 * h :]
    upper, same, lower = block_masks(folded.shape)
    flipped = jnp.transpose(folded, (0, 2, 1))
    top_left = jnp.where(upper | same, folded, flipped)
    bottom_right = jnp.where(lower, folded, jnp.where(same, corner, flipped))
    top = jnp.concatenate([top_left, top_right], axis=2)
    bottom = jnp.concatenate([jnp.transpose(top_right, (0, 2, 1)), bottom_right], axis=2)
    return jnp.concatenate([top, bottom], axis=1)


def shards(grads, weights, basis, first_moment, second_moment):
    highest = lax.Precision.HIGHEST
    fsdp = lax.axis_size("fsdp")
    tp = lax.axis_size("tp")
    width = first_moment.shape[2]
    rank_width = basis.shape[2]
    tp_bits = [(b, 2) for b in range(tp.bit_length() - 1)]
    basis_order = reverse_blocks(basis, len(tp_bits), width)

    projected_part = jnp.einsum("mfd,dmr->mfr", grads, basis_order, preferred_element_type=jnp.float32)
    half = halving_scatter(projected_part, "tp", tp, [(0, 2)])
    half = butterfly_sum(half, "tp", tp, reversed(range(1, len(tp_bits))))
    member = lax.axis_index("tp")
    own_place = 0
    for step, bit in enumerate(reversed(range(1, len(tp_bits)))):
        own_place = own_place + (((member >> bit) & 1) << step)
    own = lax.dynamic_slice_in_dim(half, own_place * width, width, 2)
    first_next, second_next, normal_half = adam_share(own, first_moment, second_moment)
    projected_half = doubling_gather(half.astype(jnp.bfloat16), "tp", tp, [(0, 2)])
    last = len(tp_bits) - 1
    normal_part = doubling_gather(normal_half, "tp", tp, list(reversed(tp_bits[:last])))

    image_part = jnp.einsum("mfd,mfr->mdr", grads, projected_half, preferred_element_type=jnp.float32)
    stages = [(0, 0), (1, 2), (3, 1)]
    chunk = halving_scatter(image_part, "fsdp", fsdp, stages)
    chunk = butterfly_sum(chunk, "fsdp", fsdp, [b for b in range(fsdp.bit_length() - 1) if b not in (0, 1, 3)])
    image = doubling_gather(chunk, "fsdp", fsdp, stages[1:])

    packed = pack_gram(jnp.einsum("mdr,mds->mrs", image, image, precision=highest))
    packed = butterfly_sum(packed, "tp", tp, range(last))
    packed_rows = packed.size // 128
    message = jnp.concatenate([packed.reshape(packed_rows, 128), normal_part.astype(jnp.float32).reshape(-1, 128)], axis=0)
    arrived = lax.ppermute(message, "tp", partner_perm(tp, last))
    gram = unpack_gram(packed + arrived[:packed_rows].reshape(packed.shape))
    other = arrived[packed_rows:].reshape(normal_part.shape).astype(jnp.bfloat16)
    high = (lax.axis_index("tp") >> last) & 1
    normal_full = jnp.concatenate([jnp.where(high == 0, normal_part, other), jnp.where(high == 0, other, normal_part)], axis=2)
    update = jnp.einsum("mfr,dmr->mfd", normal_full, basis, preferred_element_type=jnp.float32)
    weight_next = weights - LEARNING_RATE * GALORE_SCALE * update
    diagonal = lax.broadcasted_iota(jnp.int32, gram.shape, 1) == lax.broadcasted_iota(jnp.int32, gram.shape, 2)
    total = jnp.sum(jnp.where(diagonal, gram, 0.0), axis=(1, 2)) + EPSILON_NORM
    factor = jnp.sqrt(rank_width / total)
    scaled = image * factor[:, None, None]
    cross = gram * (factor * factor)[:, None, None]
    shaped = 1.5 * scaled - 0.5 * jnp.einsum("mdr,mrs->mds", scaled, cross, precision=highest)
    basis_own = (jnp.sqrt(D / rank_width) * shaped).astype(jnp.bfloat16)
    basis_next = reverse_blocks(doubling_gather(basis_own, "fsdp", fsdp, stages[:1]), len(tp_bits), width)
    return (weight_next, first_next, second_next, jnp.transpose(basis_next, (1, 0, 2)))


def solution(mesh):
    in_specs = (
        P(None, "fsdp", "tp"),
        P(None, "fsdp", "tp"),
        P("tp", None, None),
        P(None, "fsdp", "tp"),
        P(None, "fsdp", "tp"),
    )
    out_specs = (
        P(None, "fsdp", "tp"),
        P(None, "fsdp", "tp"),
        P(None, "fsdp", "tp"),
        P("tp", None, None),
    )
    return jax.shard_map(shards, mesh=mesh, in_specs=in_specs, out_specs=out_specs, check_vma=False)
```

```python
import jax
import jax.numpy as jnp
from jax import lax
from jax.sharding import PartitionSpec as P

D = 2560


BETA_FIRST = 0.9
BETA_SECOND = 0.999
BIAS_FIRST = 0.9999734386011124
BIAS_SECOND = 0.0952078528862904
EPSILON = 1e-08
EPSILON_NORM = 1e-06
LEARNING_RATE = 0.1
GALORE_SCALE = 0.25


def adam_share(grad_share, first_moment, second_moment):
    first_next = BETA_FIRST * first_moment + (1.0 - BETA_FIRST) * grad_share
    second_next = BETA_SECOND * second_moment + (1.0 - BETA_SECOND) * grad_share * grad_share
    normal = first_next / BIAS_FIRST / (jnp.sqrt(second_next / BIAS_SECOND) + EPSILON)
    return (first_next, second_next, normal.astype(jnp.bfloat16))


def partner_perm(size, bit):
    return [(i, i ^ (1 << bit)) for i in range(size)]


def butterfly_sum(value, axis, size, bits=None):
    if bits is None:
        bits = range(size.bit_length() - 1)
    for bit in bits:
        value = value + lax.ppermute(value, axis, partner_perm(size, bit))
    return value


def halving_scatter(value, axis, size, stages):
    index = lax.axis_index(axis)
    for bit, dim in stages:
        half = value.shape[dim] // 2
        mine = (index >> bit) & 1
        keep = lax.dynamic_slice_in_dim(value, mine * half, half, dim)
        send = lax.dynamic_slice_in_dim(value, (1 - mine) * half, half, dim)
        value = keep + lax.ppermute(send, axis, partner_perm(size, bit))
    return value


def doubling_gather(value, axis, size, stages):
    index = lax.axis_index(axis)
    for bit, dim in reversed(stages):
        mine = (index >> bit) & 1
        other = lax.ppermute(value, axis, partner_perm(size, bit))
        low = jnp.where(mine == 0, value, other)
        high = jnp.where(mine == 0, other, value)
        value = jnp.concatenate([low, high], axis=dim)
    return value


def reverse_blocks(value, bits, width):
    lead = value.shape[:-1]
    split = value.reshape(lead + (2,) * bits + (width,))
    axes = tuple(range(len(lead))) + tuple(len(lead) + bits - 1 - i for i in range(bits)) + (len(lead) + bits,)
    return jnp.transpose(split, axes).reshape(value.shape)


def block_masks(shape):
    rows = lax.broadcasted_iota(jnp.int32, shape, 1)
    cols = lax.broadcasted_iota(jnp.int32, shape, 2)
    return rows < cols, rows == cols, rows > cols


def pack_gram(gram):
    h = gram.shape[1] // 2
    top_left, top_right, bottom_right = gram[:, :h, :h], gram[:, :h, h:], gram[:, h:, h:]
    upper, same, lower = block_masks(top_left.shape)
    folded = jnp.where(upper | same, top_left, bottom_right)
    corner = jnp.sum(jnp.where(same, bottom_right, 0.0), axis=1, keepdims=True)
    return jnp.concatenate([folded, top_right, corner], axis=1)


def unpack_gram(packed):
    h = packed.shape[2]
    folded, top_right, corner = packed[:, :h], packed[:, h : 2 * h], packed[:, 2 * h :]
    upper, same, lower = block_masks(folded.shape)
    flipped = jnp.transpose(folded, (0, 2, 1))
    top_left = jnp.where(upper | same, folded, flipped)
    bottom_right = jnp.where(lower, folded, jnp.where(same, corner, flipped))
    top = jnp.concatenate([top_left, top_right], axis=2)
    bottom = jnp.concatenate([jnp.transpose(top_right, (0, 2, 1)), bottom_right], axis=2)
    return jnp.concatenate([top, bottom], axis=1)


def shards(grads, weights, basis, first_moment, second_moment):
    highest = lax.Precision.HIGHEST
    fsdp = lax.axis_size("fsdp")
    tp = lax.axis_size("tp")
    width = first_moment.shape[2]
    rank_width = basis.shape[2]
    tp_bits = [(b, 2) for b in range(tp.bit_length() - 1)]
    basis_order = reverse_blocks(basis, len(tp_bits), width)

    projected_part = jnp.einsum("mfd,dmr->mfr", grads, basis_order, preferred_element_type=jnp.float32)
    half = halving_scatter(projected_part, "tp", tp, [(0, 2)])
    half = butterfly_sum(half, "tp", tp, range(1, len(tp_bits)))
    member = lax.axis_index("tp")
    own_place = 0
    for step, bit in enumerate(reversed(range(1, len(tp_bits)))):
        own_place = own_place + (((member >> bit) & 1) << step)
    own = lax.dynamic_slice_in_dim(half, own_place * width, width, 2)
    first_next, second_next, normal_half = adam_share(own, first_moment, second_moment)
    projected_half = doubling_gather(half.astype(jnp.bfloat16), "tp", tp, [(0, 2)])
    normal_full = doubling_gather(normal_half, "tp", tp, list(reversed(tp_bits)))

    image_part = jnp.einsum("mfd,mfr->mdr", grads, projected_half, preferred_element_type=jnp.float32)
    stages = [(0, 0), (1, 2), (3, 1)]
    chunk = halving_scatter(image_part, "fsdp", fsdp, stages)
    chunk = butterfly_sum(chunk, "fsdp", fsdp, [b for b in range(fsdp.bit_length() - 1) if b not in (0, 1, 3)])
    image = doubling_gather(chunk, "fsdp", fsdp, stages[1:])

    update = jnp.einsum("mfr,dmr->mfd", normal_full, basis, preferred_element_type=jnp.float32)
    weight_next = weights - LEARNING_RATE * GALORE_SCALE * update

    packed = pack_gram(jnp.einsum("mdr,mds->mrs", image, image, precision=highest))
    gram = unpack_gram(butterfly_sum(packed, "tp", tp))
    diagonal = lax.broadcasted_iota(jnp.int32, gram.shape, 1) == lax.broadcasted_iota(jnp.int32, gram.shape, 2)
    total = jnp.sum(jnp.where(diagonal, gram, 0.0), axis=(1, 2)) + EPSILON_NORM
    factor = jnp.sqrt(rank_width / total)
    scaled = image * factor[:, None, None]
    cross = gram * (factor * factor)[:, None, None]
    shaped = 1.5 * scaled - 0.5 * jnp.einsum("mdr,mrs->mds", scaled, cross, precision=highest)
    basis_own = (jnp.sqrt(D / rank_width) * shaped).astype(jnp.bfloat16)
    basis_next = reverse_blocks(doubling_gather(basis_own, "fsdp", fsdp, stages[:1]), len(tp_bits), width)
    return (weight_next, first_next, second_next, jnp.transpose(basis_next, (1, 0, 2)))


def solution(mesh):
    in_specs = (
        P(None, "fsdp", "tp"),
        P(None, "fsdp", "tp"),
        P("tp", None, None),
        P(None, "fsdp", "tp"),
        P(None, "fsdp", "tp"),
    )
    out_specs = (
        P(None, "fsdp", "tp"),
        P(None, "fsdp", "tp"),
        P(None, "fsdp", "tp"),
        P("tp", None, None),
    )
    return jax.shard_map(shards, mesh=mesh, in_specs=in_specs, out_specs=out_specs, check_vma=False)
```

```python
import jax
import jax.numpy as jnp
from jax import lax
from jax.sharding import PartitionSpec as P

D = 2560


BETA_FIRST = 0.9
BETA_SECOND = 0.999
BIAS_FIRST = 0.9999734386011124
BIAS_SECOND = 0.0952078528862904
EPSILON = 1e-08
EPSILON_NORM = 1e-06
LEARNING_RATE = 0.1
GALORE_SCALE = 0.25


def adam_share(grad_share, first_moment, second_moment):
    first_next = BETA_FIRST * first_moment + (1.0 - BETA_FIRST) * grad_share
    second_next = BETA_SECOND * second_moment + (1.0 - BETA_SECOND) * grad_share * grad_share
    normal = first_next / BIAS_FIRST / (jnp.sqrt(second_next / BIAS_SECOND) + EPSILON)
    return (first_next, second_next, normal.astype(jnp.bfloat16))


def partner_perm(size, bit):
    return [(i, i ^ (1 << bit)) for i in range(size)]


def butterfly_sum(value, axis, size, bits=None):
    if bits is None:
        bits = range(size.bit_length() - 1)
    for bit in bits:
        value = value + lax.ppermute(value, axis, partner_perm(size, bit))
    return value


def halving_scatter(value, axis, size, stages):
    index = lax.axis_index(axis)
    for bit, dim in stages:
        half = value.shape[dim] // 2
        mine = (index >> bit) & 1
        keep = lax.dynamic_slice_in_dim(value, mine * half, half, dim)
        send = lax.dynamic_slice_in_dim(value, (1 - mine) * half, half, dim)
        value = keep + lax.ppermute(send, axis, partner_perm(size, bit))
    return value


def doubling_gather(value, axis, size, stages):
    index = lax.axis_index(axis)
    for bit, dim in reversed(stages):
        mine = (index >> bit) & 1
        other = lax.ppermute(value, axis, partner_perm(size, bit))
        low = jnp.where(mine == 0, value, other)
        high = jnp.where(mine == 0, other, value)
        value = jnp.concatenate([low, high], axis=dim)
    return value


def reverse_blocks(value, bits, width):
    lead = value.shape[:-1]
    split = value.reshape(lead + (2,) * bits + (width,))
    axes = tuple(range(len(lead))) + tuple(len(lead) + bits - 1 - i for i in range(bits)) + (len(lead) + bits,)
    return jnp.transpose(split, axes).reshape(value.shape)


def block_masks(shape):
    rows = lax.broadcasted_iota(jnp.int32, shape, 1)
    cols = lax.broadcasted_iota(jnp.int32, shape, 2)
    return rows < cols, rows == cols, rows > cols


def pack_gram(gram):
    h = gram.shape[1] // 2
    top_left, top_right, bottom_right = gram[:, :h, :h], gram[:, :h, h:], gram[:, h:, h:]
    upper, same, lower = block_masks(top_left.shape)
    folded = jnp.where(upper | same, top_left, bottom_right)
    corner = jnp.sum(jnp.where(same, bottom_right, 0.0), axis=1, keepdims=True)
    return jnp.concatenate([folded, top_right, corner], axis=1)


def unpack_gram(packed):
    h = packed.shape[2]
    folded, top_right, corner = packed[:, :h], packed[:, h : 2 * h], packed[:, 2 * h :]
    upper, same, lower = block_masks(folded.shape)
    flipped = jnp.transpose(folded, (0, 2, 1))
    top_left = jnp.where(upper | same, folded, flipped)
    bottom_right = jnp.where(lower, folded, jnp.where(same, corner, flipped))
    top = jnp.concatenate([top_left, top_right], axis=2)
    bottom = jnp.concatenate([jnp.transpose(top_right, (0, 2, 1)), bottom_right], axis=2)
    return jnp.concatenate([top, bottom], axis=1)


def shards(grads, weights, basis, first_moment, second_moment):
    highest = lax.Precision.HIGHEST
    fsdp = lax.axis_size("fsdp")
    tp = lax.axis_size("tp")
    width = first_moment.shape[2]
    rank_width = basis.shape[2]
    tp_bits = [(b, 2) for b in range(tp.bit_length() - 1)]
    basis_order = reverse_blocks(basis, len(tp_bits), width)

    projected_part = jnp.einsum("mfd,dmr->mfr", grads, basis_order, preferred_element_type=jnp.float32)
    half = halving_scatter(projected_part, "tp", tp, [(0, 2)])
    half = butterfly_sum(half, "tp", tp, reversed(range(1, len(tp_bits))))
    member = lax.axis_index("tp")
    own_place = 0
    for step, bit in enumerate(reversed(range(1, len(tp_bits)))):
        own_place = own_place + (((member >> bit) & 1) << step)
    own = lax.dynamic_slice_in_dim(half, own_place * width, width, 2)
    first_next, second_next, normal_half = adam_share(own, first_moment, second_moment)
    projected_half = doubling_gather(half.astype(jnp.bfloat16), "tp", tp, [(0, 2)])
    normal_full = doubling_gather(normal_half, "tp", tp, list(reversed(tp_bits)))

    image_part = jnp.einsum("mfd,mfr->mdr", grads, projected_half, preferred_element_type=jnp.float32)
    stages = [(0, 0), (1, 2), (3, 1)]
    chunk = halving_scatter(image_part, "fsdp", fsdp, stages)
    chunk = butterfly_sum(chunk, "fsdp", fsdp, [b for b in range(fsdp.bit_length() - 1) if b not in (0, 1, 3)])
    image = doubling_gather(chunk, "fsdp", fsdp, stages[1:])

    update = jnp.einsum("mfr,dmr->mfd", normal_full, basis, preferred_element_type=jnp.float32)
    weight_next = weights - LEARNING_RATE * GALORE_SCALE * update

    packed = pack_gram(jnp.einsum("mdr,mds->mrs", image, image, precision=highest))
    gram = unpack_gram(butterfly_sum(packed, "tp", tp))
    diagonal = lax.broadcasted_iota(jnp.int32, gram.shape, 1) == lax.broadcasted_iota(jnp.int32, gram.shape, 2)
    total = jnp.sum(jnp.where(diagonal, gram, 0.0), axis=(1, 2)) + EPSILON_NORM
    factor = jnp.sqrt(rank_width / total)
    scaled = image * factor[:, None, None]
    cross = gram * (factor * factor)[:, None, None]
    shaped = 1.5 * scaled - 0.5 * jnp.einsum("mdr,mrs->mds", scaled, cross, precision=highest)
    basis_own = (jnp.sqrt(D / rank_width) * shaped).astype(jnp.bfloat16)
    basis_own = jnp.transpose(reverse_blocks(basis_own, len(tp_bits), width), (1, 0, 2))
    basis_next = doubling_gather(basis_own, "fsdp", fsdp, [(0, 1)])
    return (weight_next, first_next, second_next, basis_next)


def solution(mesh):
    in_specs = (
        P(None, "fsdp", "tp"),
        P(None, "fsdp", "tp"),
        P("tp", None, None),
        P(None, "fsdp", "tp"),
        P(None, "fsdp", "tp"),
    )
    out_specs = (
        P(None, "fsdp", "tp"),
        P(None, "fsdp", "tp"),
        P(None, "fsdp", "tp"),
        P("tp", None, None),
    )
    return jax.shard_map(shards, mesh=mesh, in_specs=in_specs, out_specs=out_specs, check_vma=False)
```
